128 devices in a mesh: gx: 8 (over z, core), gy: 16 (over y, x).
Axes of the slice: x: 4, y: 4, z: 4, core: 2. Of those that a mesh axis runs over, the one named last changes fastest.
Arguments:
- initial_guess: float32 [5, 64, 512, 128], P(None, 'gx', 'gy'), may hold values from -6 to 6
- right_side: float32 [5, 64, 512, 128], P(None, 'gx', 'gy'), may hold values from -6 to 6
- coefficients: float32 [5, 64, 512, 128], P(None, 'gx', 'gy'), may hold values from 0.3 to 3
- tunnel_mask: int32 [64, 512, 128], P('gx', 'gy'), may hold values 0 or 1
- stencil: float32 [27, 5, 5], replicated, may hold values from -0.03 to 1.15, as said below
Outputs:
- fine_iterate: float32 [5, 64, 512, 128], P(None, 'gx', 'gy')
- middle_iterate: float32 [5, 32, 256, 128], P(None, 'gx', 'gy')
- lower_iterate: float32 [5, 16, 128, 128], P(None, 'gx', 'gy')
- coarse_residual: float32 [5, 8, 64, 128], P(None, 'gx', 'gy')
The draws below stay inside these ranges and needn't reach their ends.
Inputs may be any that keep to these rules, and one draw needn't show every extreme that they name: `stencil`: entries of all 27 blocks; the centre block's diagonal lies in 0.85 to 1.15; off-centre blocks have diagonal entries in -0.025 to -0.01 and off-diagonal entries in -0.004 to 0.004; the centre block's off-diagonal entries lie in -0.02 to 0.02.
All inputs are finite; a program needn't handle non-finite values. No bound on the sum of `tunnel_mask` on one device may be relied on, other than what follows from the above.
Results may differ from the reference program's by a relative error of at most 0.00029.
Values sent between devices are 32-bit elements; how exact they have to be, the bound alone decides.
No kernel may reach another device: no remote copies, remote signals or barrier semaphores. Data moves between devices by JAX's collectives and lax.ppermute only.
A program may use at most 64 MiB of HBM per device.

```python
import math
import jax
import jax.numpy as jnp
from jax import lax

COMP = 5
SWEEPS = 2
CZ = 128
NX = 64
NY = 512


def draw_stencil(key, part):
    key_off, key_link, key_centre, key_cross = jax.random.split(key, 4)
    identity = jnp.eye(COMP, dtype=jnp.float32)
    scatter_part = jax.random.uniform(key_off, (27, COMP, COMP), jnp.float32, -0.004, 0.004)
    link = -jax.random.uniform(key_link, (27, COMP), jnp.float32, 0.01, 0.025)
    blocks = scatter_part * (1.0 - identity) + link[:, :, None] * identity
    centre = jax.random.uniform(key_centre, (COMP,), jnp.float32, 0.85, 1.15)
    cross = jax.random.uniform(key_cross, (COMP, COMP), jnp.float32, -0.02, 0.02)
    centre_block = cross * (1.0 - identity) + centre[:, None] * identity
    return blocks.at[13].set(centre_block)


def set_ends(array, rng, smallest, largest):
    extent = array.shape
    index_at = [jax.random.randint(jax.random.fold_in(rng, axis), (), 0, extent[axis]) for axis in range(len(extent))]
    array = array.at[tuple(index_at)].set(smallest)
    longest = extent.index(max(extent))
    index_at[longest] = (index_at[longest] + 1) % extent[longest]
    return array.at[tuple(index_at)].set(largest)


def block_scale(key, extent, cuts, smallest, top_value):
    def one(axis_at, parts):
        draws = jax.random.uniform(jax.random.fold_in(jax.random.fold_in(key, 6), axis_at), (parts,), jnp.float32, smallest / len(cuts), top_value / len(cuts))
        return jnp.repeat(jnp.exp(draws), extent[axis_at] // parts).reshape((-1,) + (1,) * (len(extent) - axis_at - 1))

    gain = one(*cuts[0])
    for cut in cuts[1:]:
        gain = gain * one(*cut)
    return gain


def noise(key, extent, deviation, limit, cuts=(), kind=jnp.bfloat16):
    array = deviation * jax.random.normal(key, extent, jnp.float32)
    if cuts:
        array = array * block_scale(key, extent, cuts, -0.22, 0.18)
    return jnp.clip(array, -limit, limit).astype(kind)


def setup_inputs(seed: int = 0) -> dict:
    key_list = jax.random.split(jax.random.key(seed), 6)
    initial_guess = noise(key_list[0], (COMP, NX, NY, CZ), 1.0, 6.0, ((1, 8), (2, 16)), jnp.float32)
    right_side = noise(key_list[1], (COMP, NX, NY, CZ), 1.0, 6.0, ((1, 8), (2, 16)), jnp.float32)
    coefficients = jnp.clip(jnp.exp(math.log(3.0) - 2.3025851 * jax.random.uniform(key_list[2], (COMP, NX, NY, CZ), jnp.float32) ** block_scale(key_list[2], (COMP, NX, NY, CZ), ((1, 8), (2, 16)), -0.2, 0.2)), 0.3, 3.0)
    tunnel_mask = set_ends((jax.random.randint(key_list[3], (NX, NY, CZ), 0, 8) < 7).astype(jnp.int32), jax.random.fold_in(key_list[3], 1), 0, 1)
    stencil = draw_stencil(jax.random.fold_in(key_list[5], 71), 0)
    return dict(initial_guess=initial_guess, right_side=right_side, coefficients=coefficients, tunnel_mask=tunnel_mask, stencil=stencil)


DAMPING = 0.7
WEIGHTS = (0.125, 0.375, 0.375, 0.125)


def pad_plane(values):
    return jnp.pad(values, ((0, 0), (1, 1), (1, 1), (0, 0)))


def operate(iterate, conduct, rock_share, stencil, faces):
    masked = rock_share[None] * iterate
    padded = jnp.pad(faces(masked), ((0, 0), (0, 0), (0, 0), (1, 1)))
    extent_x, extent_y, extent_z = iterate.shape[1], iterate.shape[2], iterate.shape[3]
    summed = jnp.zeros(iterate.shape, jnp.float32)
    for offset in range(27):
        shift_x, shift_y, shift_z = offset // 9, (offset // 3) % 3, offset % 3
        shifted = padded[:, shift_x:shift_x + extent_x, shift_y:shift_y + extent_y, shift_z:shift_z + extent_z]
        summed = summed + jnp.einsum("ab,bxyz->axyz", stencil[offset], shifted, precision=lax.Precision.HIGHEST)
    return conduct * rock_share[None] * summed


def smooth_level(iterate, forcing, conduct, rock_share, stencil, faces):
    diagonal = conduct * jnp.diagonal(stencil[13])[:, None, None, None]
    source = rock_share[None] * forcing
    if iterate is None:
        iterate = DAMPING * source / diagonal
        remaining = SWEEPS - 1
    else:
        remaining = SWEEPS
    for sweep_index in range(remaining):
        iterate = iterate + DAMPING * (source - operate(iterate, conduct, rock_share, stencil, faces)) / diagonal
    residual = source - operate(iterate, conduct, rock_share, stencil, faces)
    return iterate, residual


def shrink(padded):
    extent_x = padded.shape[1] - 2
    along_x = sum(WEIGHTS[weight_index] * padded[:, weight_index:weight_index + extent_x - 1:2] for weight_index in range(4))
    extent_y = padded.shape[2] - 2
    return sum(WEIGHTS[weight_index] * along_x[:, :, weight_index:weight_index + extent_y - 1:2] for weight_index in range(4))


def coarsen(values):
    leading = values.shape[:-3]
    extent_x, extent_y, extent_z = values.shape[-3], values.shape[-2], values.shape[-1]
    reshaped = values.reshape(leading + (extent_x // 2, 2, extent_y // 2, 2, extent_z))
    return reshaped.mean(axis=(-4, -2))


def reference(initial_guess, right_side, coefficients, tunnel_mask, stencil):
    rock_share = tunnel_mask.astype(jnp.float32)
    conduct = coefficients
    fine_iterate, residual = smooth_level(initial_guess, right_side, conduct, rock_share, stencil, pad_plane)
    kept = [fine_iterate]
    for layer_index in range(2):
        forcing = shrink(pad_plane(residual))
        conduct = coarsen(conduct)
        rock_share = coarsen(rock_share)
        iterate, residual = smooth_level(None, forcing, conduct, rock_share, stencil, pad_plane)
        kept.append(iterate)
    forcing = shrink(pad_plane(residual))
    conduct = coarsen(conduct)
    rock_share = coarsen(rock_share)
    iterate, coarse_residual = smooth_level(None, forcing, conduct, rock_share, stencil, pad_plane)
    return kept[0], kept[1], kept[2], coarse_residual
```

```python
import jax
import jax.numpy as jnp
from jax import lax
from jax.sharding import PartitionSpec as P

COMP = 5
DAMPING = 0.7
WEIGHTS = (0.125, 0.375, 0.375, 0.125)


def exchange(block, hx, hy):
    x_size, y_size = block.shape[1], block.shape[2]
    nx, ny = lax.axis_size("gx"), lax.axis_size("gy")
    kx, ky = -(-hx // x_size), -(-hy // y_size)
    rows = []
    for dx in range(-kx, kx + 1):
        xlo, xhi = max(0, -hx - dx * x_size), min(x_size, x_size + hx - dx * x_size)
        row = []
        for dy in range(-ky, ky + 1):
            ylo, yhi = max(0, -hy - dy * y_size), min(y_size, y_size + hy - dy * y_size)
            piece = block[:, xlo:xhi, ylo:yhi]
            if dx or dy:
                pairs = [
                    ((i + dx) * ny + (j + dy), i * ny + j)
                    for i in range(nx)
                    for j in range(ny)
                    if 0 <= i + dx < nx and 0 <= j + dy < ny
                ]
                piece = lax.ppermute(piece, ("gx", "gy"), pairs)
            row.append(piece)
        rows.append(jnp.concatenate(row, axis=2))
    return jnp.concatenate(rows, axis=1)


def with_halo(block):
    for axis, dim in (("gx", 1), ("gy", 2)):
        count = lax.axis_size(axis)
        forward = [(i, i + 1) for i in range(count - 1)]
        backward = [(target, source) for source, target in forward]
        low = lax.ppermute(lax.slice_in_dim(block, block.shape[dim] - 1, None, axis=dim), axis, forward)
        high = lax.ppermute(lax.slice_in_dim(block, 0, 1, axis=dim), axis, backward)
        block = jnp.concatenate([low, block, high], axis=dim)
    return block


def operate_block(iterate, conduct, rock, stencil):
    masked = rock[None] * iterate
    summed = stencil_sum(with_halo(masked), stencil)
    return conduct * rock[None] * summed


def smooth_block(forcing, conduct, rock, stencil, sweeps):
    diagonal = conduct * jnp.diagonal(stencil[13])[:, None, None, None]
    source = rock[None] * forcing
    iterate = DAMPING * source / diagonal
    for _ in range(sweeps - 1):
        iterate = iterate + DAMPING * (source - operate_block(iterate, conduct, rock, stencil)) / diagonal
    residual = source - operate_block(iterate, conduct, rock, stencil)
    return iterate, residual


def crop(values, h):
    if h == 0:
        return values
    return values[:, h:-h, h:-h]


def stencil_sum(masked, stencil):
    padded = jnp.pad(masked, ((0, 0), (0, 0), (0, 0), (1, 1)))
    ex, ey, ez = masked.shape[1] - 2, masked.shape[2] - 2, masked.shape[3]
    acc = [None] * COMP
    for offset in range(27):
        sx, sy, sz = offset // 9, offset // 3 % 3, offset % 3
        shifted = padded[:, sx : sx + ex, sy : sy + ey, sz : sz + ez]
        for a in range(COMP):
            for b in range(COMP):
                term = stencil[offset, a, b] * shifted[b]
                acc[a] = term if acc[a] is None else acc[a] + term
    return jnp.stack(acc)


def level_chain(iterate, forcing, conduct, rock, stencil, h, sweeps):
    safe = jnp.where(conduct == 0.0, 1.0, conduct)
    diag = jnp.diagonal(stencil[13])[:, None, None, None]
    diagonal = safe * diag
    source = rock[None] * forcing
    if iterate is None:
        iterate = DAMPING * source / diagonal
        remaining = sweeps - 1
    else:
        remaining = sweeps
    for _ in range(remaining):
        masked = rock[None] * iterate
        inner = crop(safe, 1)
        applied = inner * crop_rock(rock)[None] * stencil_sum(masked, stencil)
        iterate = crop(iterate, 1) + DAMPING * (crop(source, 1) - applied) / crop(diagonal, 1)
        safe, diagonal, source, rock = inner, crop(diagonal, 1), crop(source, 1), crop_rock(rock)
    masked = rock[None] * iterate
    inner = crop(safe, 1)
    applied = inner * crop_rock(rock)[None] * stencil_sum(masked, stencil)
    residual = crop(source, 1) - applied
    return iterate, residual


def crop_rock(rock):
    return rock[1:-1, 1:-1]


def shrink(padded):
    extent_x = padded.shape[1] - 2
    along_x = sum(
        WEIGHTS[w] * padded[:, w : w + extent_x - 1 : 2] for w in range(4)
    )
    extent_y = padded.shape[2] - 2
    return sum(WEIGHTS[w] * along_x[:, :, w : w + extent_y - 1 : 2] for w in range(4))


def coarsen(values):
    leading = values.shape[:-3]
    ex, ey, ez = values.shape[-3], values.shape[-2], values.shape[-1]
    reshaped = values.reshape(leading + (ex // 2, 2, ey // 2, 2, ez))
    return reshaped.mean(axis=(-4, -2))


def body(initial_guess, right_side, coefficients, tunnel_mask, stencil):
    rock = tunnel_mask.astype(jnp.float32)
    conduct = coefficients
    h0 = 4
    packed = jnp.concatenate([initial_guess, right_side, conduct, rock[None]], axis=0)
    padded = exchange(packed, h0, h0)
    v_p, f_p, c_p, s_p = padded[0:5], padded[5:10], padded[10:15], padded[15]
    iterate, residual = level_chain(v_p, f_p, c_p, s_p, stencil, h0, 2)
    kept = [crop(iterate, 2)]
    forcing = shrink(residual)
    halos = (3, 3)
    for level in range(2):
        conduct = coarsen(conduct)
        rock = coarsen(rock)
        h = halos[level]
        packed = jnp.concatenate([forcing, conduct, rock[None]], axis=0)
        padded = exchange(packed, h, h)
        f_p, c_p, s_p = padded[0:5], padded[5:10], padded[10]
        iterate, residual = level_chain(None, f_p, c_p, s_p, stencil, h, 2)
        kept.append(crop(iterate, h - 1))
        forcing = shrink(residual)
    conduct = coarsen(conduct)
    rock = coarsen(rock)
    iterate, residual = smooth_block(forcing, conduct, rock, stencil, 2)
    kept.append(residual)
    return tuple(kept)


def solution(mesh):
    placed = (
        P(None, "gx", "gy", None),
        P(None, "gx", "gy", None),
        P(None, "gx", "gy", None),
        P("gx", "gy", None),
        P(),
    )
    return jax.shard_map(
        body,
        mesh=mesh,
        in_specs=placed,
        out_specs=(
            P(None, "gx", "gy", None),
            P(None, "gx", "gy", None),
            P(None, "gx", "gy", None),
            P(None, "gx", "gy", None),
        ),
        check_vma=False,
    )
```

```python
import jax
import jax.numpy as jnp
from jax import lax
from jax.sharding import PartitionSpec as P

DAMPING = 0.7
WEIGHTS = (0.125, 0.375, 0.375, 0.125)


def exchange(block, hx, hy):
    x_size, y_size = block.shape[1], block.shape[2]
    nx, ny = lax.axis_size("gx"), lax.axis_size("gy")
    kx, ky = -(-hx // x_size), -(-hy // y_size)
    rows = []
    for dx in range(-kx, kx + 1):
        xlo, xhi = max(0, -hx - dx * x_size), min(x_size, x_size + hx - dx * x_size)
        row = []
        for dy in range(-ky, ky + 1):
            ylo, yhi = max(0, -hy - dy * y_size), min(y_size, y_size + hy - dy * y_size)
            piece = block[:, xlo:xhi, ylo:yhi]
            if dx or dy:
                pairs = [
                    ((i + dx) * ny + (j + dy), i * ny + j)
                    for i in range(nx)
                    for j in range(ny)
                    if 0 <= i + dx < nx and 0 <= j + dy < ny
                ]
                piece = lax.ppermute(piece, ("gx", "gy"), pairs)
            row.append(piece)
        rows.append(jnp.concatenate(row, axis=2))
    return jnp.concatenate(rows, axis=1)


def with_halo(block):
    for axis, dim in (("gx", 1), ("gy", 2)):
        count = lax.axis_size(axis)
        forward = [(i, i + 1) for i in range(count - 1)]
        backward = [(target, source) for source, target in forward]
        low = lax.ppermute(lax.slice_in_dim(block, block.shape[dim] - 1, None, axis=dim), axis, forward)
        high = lax.ppermute(lax.slice_in_dim(block, 0, 1, axis=dim), axis, backward)
        block = jnp.concatenate([low, block, high], axis=dim)
    return block


def operate_block(iterate, conduct, rock, stencil):
    masked = rock[None] * iterate
    summed = stencil_sum(with_halo(masked), stencil)
    return conduct * rock[None] * summed


def smooth_block(iterate, forcing, conduct, rock, stencil, sweeps):
    diagonal = conduct * jnp.diagonal(stencil[13])[:, None, None, None]
    source = rock[None] * forcing
    if iterate is None:
        iterate = DAMPING * source / diagonal
        sweeps = sweeps - 1
    for _ in range(sweeps):
        iterate = iterate + DAMPING * (source - operate_block(iterate, conduct, rock, stencil)) / diagonal
    residual = source - operate_block(iterate, conduct, rock, stencil)
    return iterate, residual


def crop(values, h):
    if h == 0:
        return values
    return values[:, h:-h, h:-h]


def stencil_sum(masked, stencil):
    padded = jnp.pad(masked, ((0, 0), (0, 0), (0, 0), (1, 1)))
    ex, ey, ez = masked.shape[1] - 2, masked.shape[2] - 2, masked.shape[3]
    summed = jnp.zeros((masked.shape[0], ex, ey, ez), jnp.float32)
    for offset in range(27):
        sx, sy, sz = offset // 9, offset // 3 % 3, offset % 3
        shifted = padded[:, sx : sx + ex, sy : sy + ey, sz : sz + ez]
        summed = summed + jnp.einsum(
            "ab,bxyz->axyz", stencil[offset], shifted, precision=lax.Precision.HIGHEST
        )
    return summed


def level_chain(iterate, forcing, conduct, rock, stencil, h, sweeps):
    safe = jnp.where(conduct == 0.0, 1.0, conduct)
    diag = jnp.diagonal(stencil[13])[:, None, None, None]
    diagonal = safe * diag
    source = rock[None] * forcing
    if iterate is None:
        iterate = DAMPING * source / diagonal
        remaining = sweeps - 1
    else:
        remaining = sweeps
    for _ in range(remaining):
        masked = rock[None] * iterate
        inner = crop(safe, 1)
        applied = inner * crop_rock(rock)[None] * stencil_sum(masked, stencil)
        iterate = crop(iterate, 1) + DAMPING * (crop(source, 1) - applied) / crop(diagonal, 1)
        safe, diagonal, source, rock = inner, crop(diagonal, 1), crop(source, 1), crop_rock(rock)
    masked = rock[None] * iterate
    inner = crop(safe, 1)
    applied = inner * crop_rock(rock)[None] * stencil_sum(masked, stencil)
    residual = crop(source, 1) - applied
    return iterate, residual


def crop_rock(rock):
    return rock[1:-1, 1:-1]


def shrink(padded):
    extent_x = padded.shape[1] - 2
    along_x = sum(
        WEIGHTS[w] * padded[:, w : w + extent_x - 1 : 2] for w in range(4)
    )
    extent_y = padded.shape[2] - 2
    return sum(WEIGHTS[w] * along_x[:, :, w : w + extent_y - 1 : 2] for w in range(4))


def coarsen(values):
    leading = values.shape[:-3]
    ex, ey, ez = values.shape[-3], values.shape[-2], values.shape[-1]
    reshaped = values.reshape(leading + (ex // 2, 2, ey // 2, 2, ez))
    return reshaped.mean(axis=(-4, -2))


def body(initial_guess, right_side, coefficients, tunnel_mask, stencil):
    rock = tunnel_mask.astype(jnp.float32)
    conduct = coefficients
    iterate, residual = smooth_block(initial_guess, right_side, conduct, rock, stencil, 2)
    kept = [iterate]
    forcing = shrink(with_halo(residual))
    halos = (3, 3)
    for level in range(2):
        conduct = coarsen(conduct)
        rock = coarsen(rock)
        h = halos[level]
        packed = jnp.concatenate([forcing, conduct, rock[None]], axis=0)
        padded = exchange(packed, h, h)
        f_p, c_p, s_p = padded[0:5], padded[5:10], padded[10]
        iterate, residual = level_chain(None, f_p, c_p, s_p, stencil, h, 2)
        kept.append(crop(iterate, h - 1))
        forcing = shrink(residual)
    conduct = coarsen(conduct)
    rock = coarsen(rock)
    iterate, residual = smooth_block(None, forcing, conduct, rock, stencil, 2)
    kept.append(residual)
    return tuple(kept)


def solution(mesh):
    placed = (
        P(None, "gx", "gy", None),
        P(None, "gx", "gy", None),
        P(None, "gx", "gy", None),
        P("gx", "gy", None),
        P(),
    )
    return jax.shard_map(
        body,
        mesh=mesh,
        in_specs=placed,
        out_specs=(
            P(None, "gx", "gy", None),
            P(None, "gx", "gy", None),
            P(None, "gx", "gy", None),
            P(None, "gx", "gy", None),
        ),
        check_vma=False,
    )
```

```python
import jax
import jax.numpy as jnp
from jax import lax
from jax.sharding import PartitionSpec as P

SWEEPS = 2


DAMPING = 0.7
WEIGHTS = (0.125, 0.375, 0.375, 0.125)


def with_halo(block, sides, width):
    for axis, dim in sides:
        count = lax.axis_size(axis)
        forward = [(i, i + 1) for i in range(count - 1)]
        backward = [(target, source) for source, target in forward]
        low = lax.ppermute(
            lax.slice_in_dim(block, block.shape[dim] - width, None, axis=dim), axis, forward
        )
        high = lax.ppermute(lax.slice_in_dim(block, 0, width, axis=dim), axis, backward)
        block = jnp.concatenate([low, block, high], axis=dim)
    return block


def exchange(block, hx, hy):
    x_size, y_size = block.shape[1], block.shape[2]
    nx, ny = lax.axis_size("gx"), lax.axis_size("gy")
    kx, ky = -(-hx // x_size), -(-hy // y_size)
    rows = []
    for dx in range(-kx, kx + 1):
        xlo, xhi = max(0, -hx - dx * x_size), min(x_size, x_size + hx - dx * x_size)
        row = []
        for dy in range(-ky, ky + 1):
            ylo, yhi = max(0, -hy - dy * y_size), min(y_size, y_size + hy - dy * y_size)
            piece = block[:, xlo:xhi, ylo:yhi]
            if dx or dy:
                pairs = [
                    ((i + dx) * ny + (j + dy), i * ny + j)
                    for i in range(nx)
                    for j in range(ny)
                    if 0 <= i + dx < nx and 0 <= j + dy < ny
                ]
                piece = lax.ppermute(piece, ("gx", "gy"), pairs)
            row.append(piece)
        rows.append(jnp.concatenate(row, axis=2))
    return jnp.concatenate(rows, axis=1)


def face_fine(values):
    return with_halo(values, (("gx", 1), ("gy", 2)), 1)


def face_coarse(values):
    return exchange(values, 1, 1)


def face_thin(values):
    return exchange(values, 1, 1)


def face_residual(values):
    return with_halo(values, (("gx", 1), ("gy", 2)), 1)


def operate(iterate, conduct, rock_share, stencil, faces):
    masked = rock_share[None] * iterate
    padded = jnp.pad(faces(masked), ((0, 0), (0, 0), (0, 0), (1, 1)))
    extent_x, extent_y, extent_z = (iterate.shape[1], iterate.shape[2], iterate.shape[3])
    summed = jnp.zeros(iterate.shape, jnp.float32)
    for offset in range(27):
        shift_x, shift_y, shift_z = (offset // 9, offset // 3 % 3, offset % 3)
        shifted = padded[
            :,
            shift_x : shift_x + extent_x,
            shift_y : shift_y + extent_y,
            shift_z : shift_z + extent_z,
        ]
        summed = summed + jnp.einsum(
            "ab,bxyz->axyz", stencil[offset], shifted, precision=lax.Precision.HIGHEST
        )
    return conduct * rock_share[None] * summed


def smooth_level(iterate, forcing, conduct, rock_share, stencil, faces):
    diagonal = conduct * jnp.diagonal(stencil[13])[:, None, None, None]
    source = rock_share[None] * forcing
    if iterate is None:
        iterate = DAMPING * source / diagonal
        remaining = SWEEPS - 1
    else:
        remaining = SWEEPS
    for sweep_index in range(remaining):
        iterate = (
            iterate
            + DAMPING * (source - operate(iterate, conduct, rock_share, stencil, faces)) / diagonal
        )
    residual = source - operate(iterate, conduct, rock_share, stencil, faces)
    return (iterate, residual)


def shrink(padded):
    extent_x = padded.shape[1] - 2
    along_x = sum(
        (
            WEIGHTS[weight_index] * padded[:, weight_index : weight_index + extent_x - 1 : 2]
            for weight_index in range(4)
        )
    )
    extent_y = padded.shape[2] - 2
    return sum(
        (
            WEIGHTS[weight_index] * along_x[:, :, weight_index : weight_index + extent_y - 1 : 2]
            for weight_index in range(4)
        )
    )


def restrict(values):
    return shrink(face_residual(values))


def coarsen(values):
    leading = values.shape[:-3]
    extent_x, extent_y, extent_z = (values.shape[-3], values.shape[-2], values.shape[-1])
    reshaped = values.reshape(leading + (extent_x // 2, 2, extent_y // 2, 2, extent_z))
    return reshaped.mean(axis=(-4, -2))


def body(initial_guess, right_side, coefficients, tunnel_mask, stencil):
    rock_share = tunnel_mask.astype(jnp.float32)
    conduct = coefficients
    fine_iterate, residual = smooth_level(
        initial_guess, right_side, conduct, rock_share, stencil, face_fine
    )
    kept = [fine_iterate]
    for layer_index in range(2):
        forcing = restrict(residual)
        conduct = coarsen(conduct)
        rock_share = coarsen(rock_share)
        iterate, residual = smooth_level(None, forcing, conduct, rock_share, stencil, face_coarse)
        kept.append(iterate)
    forcing = restrict(residual)
    conduct = coarsen(conduct)
    rock_share = coarsen(rock_share)
    iterate, coarse_residual = smooth_level(None, forcing, conduct, rock_share, stencil, face_thin)
    return (kept[0], kept[1], kept[2], coarse_residual)


def solution(mesh):
    placed = (
        P(None, "gx", "gy", None),
        P(None, "gx", "gy", None),
        P(None, "gx", "gy", None),
        P("gx", "gy", None),
        P(),
    )
    return jax.shard_map(
        body,
        mesh=mesh,
        in_specs=placed,
        out_specs=(
            P(None, "gx", "gy", None),
            P(None, "gx", "gy", None),
            P(None, "gx", "gy", None),
            P(None, "gx", "gy", None),
        ),
        check_vma=False,
    )
```

```python
import jax
import jax.numpy as jnp
from jax import lax
from jax.sharding import PartitionSpec as P

SWEEPS = 2


DAMPING = 0.7
WEIGHTS = (0.125, 0.375, 0.375, 0.125)


def with_halo(block, sides, width):
    for axis, dim in sides:
        count = lax.axis_size(axis)
        forward = [(i, i + 1) for i in range(count - 1)]
        backward = [(target, source) for source, target in forward]
        low = lax.ppermute(
            lax.slice_in_dim(block, block.shape[dim] - width, None, axis=dim), axis, forward
        )
        high = lax.ppermute(lax.slice_in_dim(block, 0, width, axis=dim), axis, backward)
        block = jnp.concatenate([low, block, high], axis=dim)
    return block


def face_fine(values):
    return with_halo(values, (("gx", 1), ("gy", 2)), 1)


def face_coarse(values):
    return with_halo(values, (("gx", 1), ("gy", 2)), 1)


def face_thin(values):
    return with_halo(values, (("gx", 1), ("gy", 2)), 1)


def face_residual(values):
    return with_halo(values, (("gx", 1), ("gy", 2)), 1)


def operate(iterate, conduct, rock_share, stencil, faces):
    masked = rock_share[None] * iterate
    padded = jnp.pad(faces(masked), ((0, 0), (0, 0), (0, 0), (1, 1)))
    extent_x, extent_y, extent_z = (iterate.shape[1], iterate.shape[2], iterate.shape[3])
    summed = jnp.zeros(iterate.shape, jnp.float32)
    for offset in range(27):
        shift_x, shift_y, shift_z = (offset // 9, offset // 3 % 3, offset % 3)
        shifted = padded[
            :,
            shift_x : shift_x + extent_x,
            shift_y : shift_y + extent_y,
            shift_z : shift_z + extent_z,
        ]
        summed = summed + jnp.einsum(
            "ab,bxyz->axyz", stencil[offset], shifted, precision=lax.Precision.HIGH
        )
    return conduct * rock_share[None] * summed


def smooth_level(iterate, forcing, conduct, rock_share, stencil, faces):
    diagonal = conduct * jnp.diagonal(stencil[13])[:, None, None, None]
    source = rock_share[None] * forcing
    if iterate is None:
        iterate = DAMPING * source / diagonal
        remaining = SWEEPS - 1
    else:
        remaining = SWEEPS
    for sweep_index in range(remaining):
        iterate = (
            iterate
            + DAMPING * (source - operate(iterate, conduct, rock_share, stencil, faces)) / diagonal
        )
    residual = source - operate(iterate, conduct, rock_share, stencil, faces)
    return (iterate, residual)


def shrink(padded):
    extent_x = padded.shape[1] - 2
    along_x = sum(
        (
            WEIGHTS[weight_index] * padded[:, weight_index : weight_index + extent_x - 1 : 2]
            for weight_index in range(4)
        )
    )
    extent_y = padded.shape[2] - 2
    return sum(
        (
            WEIGHTS[weight_index] * along_x[:, :, weight_index : weight_index + extent_y - 1 : 2]
            for weight_index in range(4)
        )
    )


def restrict(values):
    return shrink(face_residual(values))


def coarsen(values):
    leading = values.shape[:-3]
    extent_x, extent_y, extent_z = (values.shape[-3], values.shape[-2], values.shape[-1])
    reshaped = values.reshape(leading + (extent_x // 2, 2, extent_y // 2, 2, extent_z))
    return reshaped.mean(axis=(-4, -2))


def body(initial_guess, right_side, coefficients, tunnel_mask, stencil):
    rock_share = tunnel_mask.astype(jnp.float32)
    conduct = coefficients
    fine_iterate, residual = smooth_level(
        initial_guess, right_side, conduct, rock_share, stencil, face_fine
    )
    kept = [fine_iterate]
    for layer_index in range(2):
        forcing = restrict(residual)
        conduct = coarsen(conduct)
        rock_share = coarsen(rock_share)
        iterate, residual = smooth_level(None, forcing, conduct, rock_share, stencil, face_coarse)
        kept.append(iterate)
    forcing = restrict(residual)
    conduct = coarsen(conduct)
    rock_share = coarsen(rock_share)
    iterate, coarse_residual = smooth_level(None, forcing, conduct, rock_share, stencil, face_thin)
    return (kept[0], kept[1], kept[2], coarse_residual)


def solution(mesh):
    placed = (
        P(None, "gx", "gy", None),
        P(None, "gx", "gy", None),
        P(None, "gx", "gy", None),
        P("gx", "gy", None),
        P(),
    )
    return jax.shard_map(
        body,
        mesh=mesh,
        in_specs=placed,
        out_specs=(
            P(None, "gx", "gy", None),
            P(None, "gx", "gy", None),
            P(None, "gx", "gy", None),
            P(None, "gx", "gy", None),
        ),
        check_vma=False,
    )
```
